512 devices in a mesh: rx: 8 (over y), tm: 16 (over z, core), bin: 4 (over x).
Axes of the slice: x: 4, y: 8, z: 8, core: 2. Of those that a mesh axis runs over, the one named last changes fastest.
Arguments:
- samples: bfloat16 [4, 4096, 4096], P('bin', 'tm', 'rx'), may hold values from -45 to 45, as said below
- test_matrix: bfloat16 [4, 4096, 512], P('bin', 'tm'), may hold values from -0.09375 to 0.09375
- forgetting: float32 [4, 16, 512], P('bin', 'tm'), may hold values from 0 to 1, as said below
- prior_sketch: bfloat16 [4, 4096, 512], P('bin', 'rx'), may hold values from -6 to 6
Outputs:
- basis: bfloat16 [4, 16, 4096, 512], P('bin', 'tm', 'rx')
- coefficients: float32 [4, 4096, 512], P('bin', 'tm')
The draws below stay inside these ranges and needn't reach their ends.
Inputs may be any that keep to these rules, and one draw needn't show every extreme that they name: `samples`: real-valued data. `forgetting`: positive factors.
All inputs are finite; a program needn't handle non-finite values.
Results may differ from the reference program's by a relative error of at most 0.015.
Values may be sent and summed in bfloat16 or wider, within the bound.
No kernel may reach another device: no remote copies, remote signals or barrier semaphores. Data moves between devices by JAX's collectives and lax.ppermute only.
A program may use at most 64 MiB of HBM per device.

```python
import math
import jax
import jax.numpy as jnp
from jax import lax

K = 512
COL_DEV = 256
SPECTRAL_CELLS = 4
EPOCH_SEGMENTS = 16
M = 4096
COLS = 4096


def draw_samples(key, part):
    key_rows, key_cols, key_base = jax.random.split(key, 3)
    row_gain = jnp.exp(jax.random.uniform(key_rows, (SPECTRAL_CELLS, 1, M), jnp.float32, math.log(0.3), math.log(3.0)))
    col_gain = jnp.exp(jax.random.uniform(key_cols, (SPECTRAL_CELLS, COLS, 1), jnp.float32, math.log(0.3), math.log(3.0)))
    base = jnp.clip(jax.random.normal(key_base, (SPECTRAL_CELLS, COLS, M), jnp.float32), -5.0, 5.0)
    return (row_gain * col_gain * base).astype(jnp.bfloat16)


def draw_forgetting(key, part):
    attenuation_speed_seed, angular_perturbation_seed, impulsive_disturbance_seed, erasure_indicator_seed = jax.random.split(key, 4)
    attenuation_speed = jnp.exp(jax.random.uniform(attenuation_speed_seed, (SPECTRAL_CELLS, 1, K), jnp.float32, math.log(0.1), math.log(40.0)))
    angular_perturbation = jax.random.uniform(angular_perturbation_seed, (SPECTRAL_CELLS, EPOCH_SEGMENTS, K), jnp.float32, 0.5, 1.5)
    impulsive_disturbance = jax.random.uniform(impulsive_disturbance_seed, (SPECTRAL_CELLS, EPOCH_SEGMENTS, 1), jnp.float32) < 0.15
    erasure_indicator = jax.random.uniform(erasure_indicator_seed, (SPECTRAL_CELLS, EPOCH_SEGMENTS, K), jnp.float32, 0.5, 0.8)
    return jnp.exp(-attenuation_speed * angular_perturbation / EPOCH_SEGMENTS) * jnp.where(impulsive_disturbance, erasure_indicator, 1.0)


def shard_levels(stream_key, dims, cuts, low, top_value):
    factor_of = 1.0
    for dim, blocks in cuts:
        draws = jax.random.uniform(jax.random.fold_in(jax.random.fold_in(stream_key, 6), dim), (blocks,), jnp.float32, low / len(cuts), top_value / len(cuts))
        factor_of = factor_of * jnp.repeat(jnp.exp(draws), dims[dim] // blocks).reshape((-1,) + (1,) * (len(dims) - 1 - dim))
    return factor_of


def normal_values(own_key, dims, width, reach, shards=(), held_as=jnp.bfloat16):
    result = width * jax.random.normal(own_key, dims, jnp.float32)
    if shards:
        result = result * shard_levels(own_key, dims, shards, -0.22, 0.18)
    return jnp.clip(result, -reach, reach).astype(held_as)


def setup_inputs(seed: int = 0) -> dict:
    streams_of = jax.random.split(jax.random.key(seed), 5)
    samples = draw_samples(jax.random.fold_in(streams_of[4], 71), 0)
    test_matrix = normal_values(streams_of[1], (SPECTRAL_CELLS, COLS, K), COLS ** -0.5, 0.09375, ((0, 4), (1, 16)))
    forgetting = draw_forgetting(jax.random.fold_in(streams_of[4], 71), 0)
    prior_sketch = normal_values(streams_of[3], (SPECTRAL_CELLS, M, K), 1.0, 6.0, ((0, 4), (1, 8)))
    return dict(samples=samples, test_matrix=test_matrix, forgetting=forgetting, prior_sketch=prior_sketch)


def lower_solve(factor, mixed):
    return jax.scipy.linalg.solve_triangular(factor, mixed.T, lower=True).T

def reference(samples, test_matrix, forgetting, prior_sketch):
    prefix = prior_sketch.astype(jnp.float32)
    bases = []
    coords = []
    for owner in range(EPOCH_SEGMENTS):
        block = samples[:, owner * COL_DEV:(owner + 1) * COL_DEV, :].astype(jnp.float32)
        tests = test_matrix[:, owner * COL_DEV:(owner + 1) * COL_DEV, :].astype(jnp.float32)
        part = jnp.einsum('bcm,bck->bmk', block, tests, precision=lax.Precision.HIGHEST)
        prefix = forgetting[:, owner, None, :] * prefix + part
        zero_bin = jnp.zeros((1, M, K), jnp.float32)
        below = jnp.concatenate([zero_bin, prefix[:-1]], axis=0)
        above = jnp.concatenate([prefix[1:], zero_bin], axis=0)
        mixed = prefix + 0.25 * (below + above)
        gram = jnp.einsum('bmk,bml->bkl', mixed, mixed, precision=lax.Precision.HIGHEST)
        factor = jnp.linalg.cholesky(gram)
        ortho = jax.vmap(lower_solve)(factor, mixed)
        bases.append((math.sqrt(M) * ortho).astype(jnp.bfloat16))
        coords.append(jnp.einsum('bcm,bmk->bck', block, ortho, precision=lax.Precision.HIGHEST))
    return (jnp.stack(bases, axis=1), jnp.concatenate(coords, axis=1))
```

```python
import math

import jax
import jax.numpy as jnp
from jax import lax
from jax.sharding import PartitionSpec as P


def prefix_2(part, axis, combine, identity):
    place = lax.axis_index(axis)
    gathered = jax.tree.map(lambda a: lax.all_gather(a, axis), part)
    state = jax.tree.map(lambda a, e: jnp.zeros_like(a) + jnp.asarray(e, a.dtype), part, identity)

    def one(hop, state):
        return combine(
            state, jax.tree.map(lambda a: lax.dynamic_index_in_dim(a, hop, 0, False), gathered)
        )

    return lax.fori_loop(0, place, one, state)


def with_halo(block, sides, width):
    for axis, dim in sides:
        count = lax.axis_size(axis)
        forward = [(i, i + 1) for i in range(count - 1)]
        backward = [(target, source) for source, target in forward]
        low = lax.ppermute(
            lax.slice_in_dim(block, block.shape[dim] - width, None, axis=dim), axis, forward
        )
        high = lax.ppermute(lax.slice_in_dim(block, 0, width, axis=dim), axis, backward)
        block = jnp.concatenate([low, block, high], axis=dim)
    return block


def combine(earlier, later):
    return (earlier[0] * later[0], later[0][None, :] * earlier[1] + later[1])


def sketch_of(block_data, block_test):
    return lax.dot_general(
        block_data, block_test, (((0,), (0,)), ((), ())), preferred_element_type=jnp.float32
    )


def body(samples, test_matrix, forgetting, prior_sketch):
    block_data = samples[0]
    block_test = test_matrix[0]
    own_decay = forgetting[0, 0]
    prior_rows = prior_sketch[0].astype(jnp.float32)
    width = block_test.shape[1]
    rows = block_data.shape[1]
    sketch = sketch_of(block_data, block_test)
    identity = (jnp.ones((width,), jnp.float32), jnp.zeros((rows, width), jnp.float32))
    before_decay, before_sum = prefix_2((own_decay, sketch), "tm", combine, identity)
    prefix = (
        own_decay[None, :] * before_sum + sketch + (before_decay * own_decay)[None, :] * prior_rows
    )
    padded = with_halo(prefix[None], (("bin", 0),), 1)
    mixed = padded[1] + 0.25 * (padded[0] + padded[2])
    local_gram = lax.dot_general(
        mixed,
        mixed,
        (((0,), (0,)), ((), ())),
        precision=lax.Precision.HIGHEST,
        preferred_element_type=jnp.float32,
    )
    local_proj = jnp.dot(
        block_data.astype(jnp.float32),
        mixed,
        precision=lax.Precision.HIGHEST,
        preferred_element_type=jnp.float32,
    )
    summed = lax.psum(jnp.concatenate([local_gram, local_proj], axis=0), "rx")
    gram = summed[:width]
    factor = jnp.linalg.cholesky(gram)
    solved = jax.scipy.linalg.solve_triangular(
        factor, jnp.concatenate([mixed, summed[width:]], axis=0).T, lower=True
    ).T
    ortho = solved[:rows]
    coords = solved[rows:]
    receivers = rows * lax.axis_size("rx")
    basis = (math.sqrt(receivers) * ortho).astype(jnp.bfloat16)
    return (basis[None, None], coords[None])


def solution(mesh):
    return jax.shard_map(
        body,
        mesh=mesh,
        in_specs=(
            P("bin", "tm", "rx"),
            P("bin", "tm", None),
            P("bin", "tm", None),
            P("bin", "rx", None),
        ),
        out_specs=(P("bin", "tm", "rx", None), P("bin", "tm", None)),
        check_vma=False,
    )
```

```python
import math

import jax
import jax.numpy as jnp
from jax import lax
from jax.sharding import PartitionSpec as P


def prefix_2(part, axis, combine, identity):
    place = lax.axis_index(axis)
    gathered = jax.tree.map(lambda a: lax.all_gather(a, axis), part)
    state = jax.tree.map(lambda a, e: jnp.zeros_like(a) + jnp.asarray(e, a.dtype), part, identity)

    def one(hop, state):
        return combine(
            state, jax.tree.map(lambda a: lax.dynamic_index_in_dim(a, hop, 0, False), gathered)
        )

    return lax.fori_loop(0, place, one, state)


def with_halo(block, sides, width):
    for axis, dim in sides:
        count = lax.axis_size(axis)
        forward = [(i, i + 1) for i in range(count - 1)]
        backward = [(target, source) for source, target in forward]
        low = lax.ppermute(
            lax.slice_in_dim(block, block.shape[dim] - width, None, axis=dim), axis, forward
        )
        high = lax.ppermute(lax.slice_in_dim(block, 0, width, axis=dim), axis, backward)
        block = jnp.concatenate([low, block, high], axis=dim)
    return block


def combine(earlier, later):
    return (earlier[0] * later[0], later[0][None, :] * earlier[1] + later[1])


def sketch_of(block_data, block_test):
    return lax.dot_general(
        block_data, block_test, (((0,), (0,)), ((), ())), preferred_element_type=jnp.float32
    )


def body(samples, test_matrix, forgetting, prior_sketch):
    block_data = samples[0]
    block_test = test_matrix[0]
    own_decay = forgetting[0, 0]
    prior_rows = prior_sketch[0].astype(jnp.float32)
    width = block_test.shape[1]
    rows = block_data.shape[1]
    steps = lax.axis_size("tm")
    place = lax.axis_index("tm")
    gathered = lax.all_gather(
        jnp.concatenate([block_data, block_test], axis=1), "tm", axis=0, tiled=True
    )
    all_data = gathered[:, :rows]
    all_test = gathered[:, rows:]
    decays = lax.all_gather(own_decay, "tm", axis=0)
    owner = lax.broadcasted_iota(jnp.int32, (steps, steps, 1), 0)
    later = lax.broadcasted_iota(jnp.int32, (steps, steps, 1), 1)
    inside = (later > owner) & (later <= place)
    weight = jnp.prod(jnp.where(inside, decays[None], 1.0), axis=1)
    weight = jnp.where(owner[:, 0] <= place, weight, 0.0)
    prior_weight = jnp.prod(jnp.where(later[0] <= place, decays, 1.0), axis=0)
    cols = block_test.shape[0]
    scaled = (all_test.reshape(steps, cols, width).astype(jnp.float32) * weight[:, None, :]).reshape(
        steps * cols, width
    )
    high = scaled.astype(jnp.bfloat16)
    low = (scaled - high.astype(jnp.float32)).astype(jnp.bfloat16)
    both = lax.dot_general(
        all_data,
        jnp.concatenate([high, low], axis=1),
        (((0,), (0,)), ((), ())),
        preferred_element_type=jnp.float32,
    )
    prefix = both[:, :width] + both[:, width:] + prior_weight[None, :] * prior_rows
    padded = with_halo(prefix[None], (("bin", 0),), 1)
    mixed = padded[1] + 0.25 * (padded[0] + padded[2])
    local_gram = lax.dot_general(
        mixed,
        mixed,
        (((0,), (0,)), ((), ())),
        precision=lax.Precision.HIGHEST,
        preferred_element_type=jnp.float32,
    )
    local_proj = jnp.dot(
        block_data.astype(jnp.float32),
        mixed,
        precision=lax.Precision.HIGHEST,
        preferred_element_type=jnp.float32,
    )
    summed = lax.psum(jnp.concatenate([local_gram, local_proj], axis=0), "rx")
    gram = summed[:width]
    factor = jnp.linalg.cholesky(gram)
    solved = jax.scipy.linalg.solve_triangular(
        factor, jnp.concatenate([mixed, summed[width:]], axis=0).T, lower=True
    ).T
    ortho = solved[:rows]
    coords = solved[rows:]
    receivers = rows * lax.axis_size("rx")
    basis = (math.sqrt(receivers) * ortho).astype(jnp.bfloat16)
    return (basis[None, None], coords[None])


def solution(mesh):
    return jax.shard_map(
        body,
        mesh=mesh,
        in_specs=(
            P("bin", "tm", "rx"),
            P("bin", "tm", None),
            P("bin", "tm", None),
            P("bin", "rx", None),
        ),
        out_specs=(P("bin", "tm", "rx", None), P("bin", "tm", None)),
        check_vma=False,
    )
```

```python
import math

import jax
import jax.numpy as jnp
from jax import lax
from jax.sharding import PartitionSpec as P


def prefix_2(part, axis, combine, identity):
    place = lax.axis_index(axis)
    gathered = jax.tree.map(lambda a: lax.all_gather(a, axis), part)
    state = jax.tree.map(lambda a, e: jnp.zeros_like(a) + jnp.asarray(e, a.dtype), part, identity)

    def one(hop, state):
        return combine(
            state, jax.tree.map(lambda a: lax.dynamic_index_in_dim(a, hop, 0, False), gathered)
        )

    return lax.fori_loop(0, place, one, state)


def with_halo(block, sides, width):
    for axis, dim in sides:
        count = lax.axis_size(axis)
        forward = [(i, i + 1) for i in range(count - 1)]
        backward = [(target, source) for source, target in forward]
        low = lax.ppermute(
            lax.slice_in_dim(block, block.shape[dim] - width, None, axis=dim), axis, forward
        )
        high = lax.ppermute(lax.slice_in_dim(block, 0, width, axis=dim), axis, backward)
        block = jnp.concatenate([low, block, high], axis=dim)
    return block


def blocked_factor(gram, block):
    size = gram.shape[0]
    count = size // block
    hi = lax.Precision.HIGHEST
    eye = jnp.eye(block, dtype=gram.dtype)
    columns = []
    inverses = []
    for j in range(count):
        top, end = j * block, (j + 1) * block
        panel = gram[top:, top:end]
        if j:
            done = jnp.concatenate([c[top - c_top:] for c_top, c in columns], axis=1)
            panel = panel - jnp.dot(done, done[:block].T, precision=hi)
        diag = lax.linalg.cholesky(panel[:block], symmetrize_input=True)
        inverse = jnp.tril(lax.linalg.triangular_solve(diag, eye, left_side=True, lower=True))
        inverses.append(inverse)
        if j + 1 < count:
            below = jnp.dot(panel[block:], inverse.T, precision=hi)
            columns.append((top, jnp.concatenate([diag, below], axis=0)))
        else:
            columns.append((top, diag))
    return columns, inverses


def right_solve(values, columns, inverses, block):
    hi = lax.Precision.HIGHEST
    parts = []
    for j, inverse in enumerate(inverses):
        top = j * block
        part = values[:, top:top + block]
        for k in range(j):
            c_top, col = columns[k]
            part = part - jnp.dot(parts[k], col[top - c_top:top - c_top + block].T, precision=hi)
        parts.append(jnp.dot(part, inverse.T, precision=hi))
    return jnp.concatenate(parts, axis=1)


def combine(earlier, later):
    return (earlier[0] * later[0], later[0][None, :] * earlier[1] + later[1])


def sketch_of(block_data, block_test):
    return lax.dot_general(
        block_data, block_test, (((0,), (0,)), ((), ())), preferred_element_type=jnp.float32
    )


def body(samples, test_matrix, forgetting, prior_sketch):
    block_data = samples[0]
    block_test = test_matrix[0]
    own_decay = forgetting[0, 0]
    prior_rows = prior_sketch[0].astype(jnp.float32)
    width = block_test.shape[1]
    rows = block_data.shape[1]
    steps = lax.axis_size("tm")
    place = lax.axis_index("tm")
    gathered = lax.all_gather(
        jnp.concatenate([block_data, block_test], axis=1), "tm", axis=0, tiled=True
    )
    all_data = gathered[:, :rows]
    all_test = gathered[:, rows:]
    decays = lax.all_gather(own_decay, "tm", axis=0)
    owner = lax.broadcasted_iota(jnp.int32, (steps, steps, 1), 0)
    later = lax.broadcasted_iota(jnp.int32, (steps, steps, 1), 1)
    inside = (later > owner) & (later <= place)
    weight = jnp.prod(jnp.where(inside, decays[None], 1.0), axis=1)
    weight = jnp.where(owner[:, 0] <= place, weight, 0.0)
    prior_weight = jnp.prod(jnp.where(later[0] <= place, decays, 1.0), axis=0)
    cols = block_test.shape[0]
    scaled = (all_test.reshape(steps, cols, width).astype(jnp.float32) * weight[:, None, :]).reshape(
        steps * cols, width
    )
    high = scaled.astype(jnp.bfloat16)
    low = (scaled - high.astype(jnp.float32)).astype(jnp.bfloat16)
    both = lax.dot_general(
        all_data,
        jnp.concatenate([high, low], axis=1),
        (((0,), (0,)), ((), ())),
        preferred_element_type=jnp.float32,
    )
    prefix = both[:, :width] + both[:, width:] + prior_weight[None, :] * prior_rows
    padded = with_halo(prefix[None], (("bin", 0),), 1)
    mixed = padded[1] + 0.25 * (padded[0] + padded[2])
    local_gram = lax.dot_general(
        mixed,
        mixed,
        (((0,), (0,)), ((), ())),
        precision=lax.Precision.HIGHEST,
        preferred_element_type=jnp.float32,
    )
    local_proj = jnp.dot(
        block_data.astype(jnp.float32),
        mixed,
        precision=lax.Precision.HIGHEST,
        preferred_element_type=jnp.float32,
    )
    summed = lax.psum(jnp.concatenate([local_gram, local_proj], axis=0), "rx")
    gram = summed[:width]
    block = 128
    columns, inverses = blocked_factor(gram, block)
    solved = right_solve(
        jnp.concatenate([mixed, summed[width:]], axis=0), columns, inverses, block
    )
    ortho = solved[:rows]
    coords = solved[rows:]
    receivers = rows * lax.axis_size("rx")
    basis = (math.sqrt(receivers) * ortho).astype(jnp.bfloat16)
    return (basis[None, None], coords[None])


def solution(mesh):
    return jax.shard_map(
        body,
        mesh=mesh,
        in_specs=(
            P("bin", "tm", "rx"),
            P("bin", "tm", None),
            P("bin", "tm", None),
            P("bin", "rx", None),
        ),
        out_specs=(P("bin", "tm", "rx", None), P("bin", "tm", None)),
        check_vma=False,
    )
```

```python
import math

import jax
import jax.numpy as jnp
from jax import lax
from jax.sharding import PartitionSpec as P


def prefix_2(part, axis, combine, identity):
    place = lax.axis_index(axis)
    gathered = jax.tree.map(lambda a: lax.all_gather(a, axis), part)
    state = jax.tree.map(lambda a, e: jnp.zeros_like(a) + jnp.asarray(e, a.dtype), part, identity)

    def one(hop, state):
        return combine(
            state, jax.tree.map(lambda a: lax.dynamic_index_in_dim(a, hop, 0, False), gathered)
        )

    return lax.fori_loop(0, place, one, state)


def with_halo(block, sides, width):
    for axis, dim in sides:
        count = lax.axis_size(axis)
        forward = [(i, i + 1) for i in range(count - 1)]
        backward = [(target, source) for source, target in forward]
        low = lax.ppermute(
            lax.slice_in_dim(block, block.shape[dim] - width, None, axis=dim), axis, forward
        )
        high = lax.ppermute(lax.slice_in_dim(block, 0, width, axis=dim), axis, backward)
        block = jnp.concatenate([low, block, high], axis=dim)
    return block


def blocked_factor(gram, block):
    size = gram.shape[0]
    count = size // block
    hi = lax.Precision.HIGHEST
    eye = jnp.eye(block, dtype=gram.dtype)
    columns = []
    inverses = []
    for j in range(count):
        top, end = j * block, (j + 1) * block
        panel = gram[top:, top:end]
        if j:
            done = jnp.concatenate([c[top - c_top:] for c_top, c in columns], axis=1)
            panel = panel - jnp.dot(done, done[:block].T, precision=hi)
        diag = lax.linalg.cholesky(panel[:block], symmetrize_input=True)
        inverse = jnp.tril(lax.linalg.triangular_solve(diag, eye, left_side=True, lower=True))
        inverses.append(inverse)
        if j + 1 < count:
            below = jnp.dot(panel[block:], inverse.T, precision=hi)
            columns.append((top, jnp.concatenate([diag, below], axis=0)))
        else:
            columns.append((top, diag))
    return columns, inverses


def right_solve(values, columns, inverses, block):
    hi = lax.Precision.HIGHEST
    parts = []
    for j, inverse in enumerate(inverses):
        top = j * block
        part = values[:, top:top + block]
        for k in range(j):
            c_top, col = columns[k]
            part = part - jnp.dot(parts[k], col[top - c_top:top - c_top + block].T, precision=hi)
        parts.append(jnp.dot(part, inverse.T, precision=hi))
    return jnp.concatenate(parts, axis=1)


def combine(earlier, later):
    return (earlier[0] * later[0], later[0][None, :] * earlier[1] + later[1])


def sketch_of(block_data, block_test):
    return lax.dot_general(
        block_data, block_test, (((0,), (0,)), ((), ())), preferred_element_type=jnp.float32
    )


def body(samples, test_matrix, forgetting, prior_sketch):
    block_data = samples[0]
    block_test = test_matrix[0]
    own_decay = forgetting[0, 0]
    prior_rows = prior_sketch[0].astype(jnp.float32)
    width = block_test.shape[1]
    rows = block_data.shape[1]
    steps = lax.axis_size("tm")
    place = lax.axis_index("tm")
    gathered = lax.all_gather(
        jnp.concatenate([block_data, block_test], axis=1), "tm", axis=0, tiled=True
    )
    all_data = gathered[:, :rows]
    all_test = gathered[:, rows:]
    decays = lax.all_gather(own_decay, "tm", axis=0)
    owner = lax.broadcasted_iota(jnp.int32, (steps, steps, 1), 0)
    later = lax.broadcasted_iota(jnp.int32, (steps, steps, 1), 1)
    inside = (later > owner) & (later <= place)
    weight = jnp.prod(jnp.where(inside, decays[None], 1.0), axis=1)
    weight = jnp.where(owner[:, 0] <= place, weight, 0.0)
    prior_weight = jnp.prod(jnp.where(later[0] <= place, decays, 1.0), axis=0)
    cols = block_test.shape[0]
    scaled = (all_test.reshape(steps, cols, width).astype(jnp.float32) * weight[:, None, :]).reshape(
        steps * cols, width
    )
    rounded = lax.reduce_precision(scaled, exponent_bits=8, mantissa_bits=7)
    high = rounded.astype(jnp.bfloat16)
    low = (scaled - rounded).astype(jnp.bfloat16)
    both = lax.dot_general(
        all_data,
        jnp.concatenate([high, low], axis=1),
        (((0,), (0,)), ((), ())),
        preferred_element_type=jnp.float32,
    )
    prefix = both[:, :width] + both[:, width:] + prior_weight[None, :] * prior_rows
    bins = lax.axis_size("bin")
    upward = [(i, i + 1) for i in range(bins - 1)]
    downward = [(b, a) for a, b in upward]
    sent = prefix.astype(jnp.bfloat16)
    below = lax.ppermute(sent, "bin", upward).astype(jnp.float32)
    above = lax.ppermute(sent, "bin", downward).astype(jnp.float32)
    mixed = prefix + 0.25 * (below + above)
    local_gram = lax.dot_general(
        mixed,
        mixed,
        (((0,), (0,)), ((), ())),
        precision=lax.Precision.HIGHEST,
        preferred_element_type=jnp.float32,
    )
    local_proj = jnp.dot(
        block_data.astype(jnp.float32),
        mixed,
        precision=lax.Precision.HIGHEST,
        preferred_element_type=jnp.float32,
    )
    summed = lax.psum(jnp.concatenate([local_gram, local_proj], axis=0), "rx")
    gram = summed[:width]
    block = 128
    columns, inverses = blocked_factor(gram, block)
    solved = right_solve(
        jnp.concatenate([mixed, summed[width:]], axis=0), columns, inverses, block
    )
    ortho = solved[:rows]
    coords = solved[rows:]
    receivers = rows * lax.axis_size("rx")
    basis = (math.sqrt(receivers) * ortho).astype(jnp.bfloat16)
    return (basis[None, None], coords[None])


def solution(mesh):
    return jax.shard_map(
        body,
        mesh=mesh,
        in_specs=(
            P("bin", "tm", "rx"),
            P("bin", "tm", None),
            P("bin", "tm", None),
            P("bin", "rx", None),
        ),
        out_specs=(P("bin", "tm", "rx", None), P("bin", "tm", None)),
        check_vma=False,
    )
```

```python
import math

import jax
import jax.numpy as jnp
from jax import lax
from jax.sharding import PartitionSpec as P


def prefix_2(part, axis, combine, identity):
    place = lax.axis_index(axis)
    gathered = jax.tree.map(lambda a: lax.all_gather(a, axis), part)
    state = jax.tree.map(lambda a, e: jnp.zeros_like(a) + jnp.asarray(e, a.dtype), part, identity)

    def one(hop, state):
        return combine(
            state, jax.tree.map(lambda a: lax.dynamic_index_in_dim(a, hop, 0, False), gathered)
        )

    return lax.fori_loop(0, place, one, state)


def with_halo(block, sides, width):
    for axis, dim in sides:
        count = lax.axis_size(axis)
        forward = [(i, i + 1) for i in range(count - 1)]
        backward = [(target, source) for source, target in forward]
        low = lax.ppermute(
            lax.slice_in_dim(block, block.shape[dim] - width, None, axis=dim), axis, forward
        )
        high = lax.ppermute(lax.slice_in_dim(block, 0, width, axis=dim), axis, backward)
        block = jnp.concatenate([low, block, high], axis=dim)
    return block


def blocked_factor(gram, block):
    size = gram.shape[0]
    count = size // block
    hi = lax.Precision.HIGHEST
    eye = jnp.eye(block, dtype=gram.dtype)
    columns = []
    inverses = []
    for j in range(count):
        top, end = j * block, (j + 1) * block
        panel = gram[top:, top:end]
        if j:
            done = jnp.concatenate([c[top - c_top:] for c_top, c in columns], axis=1)
            panel = panel - jnp.dot(done, done[:block].T, precision=hi)
        diag = lax.linalg.cholesky(panel[:block], symmetrize_input=True)
        inverse = jnp.tril(lax.linalg.triangular_solve(diag, eye, left_side=True, lower=True))
        inverses.append(inverse)
        if j + 1 < count:
            below = jnp.dot(panel[block:], inverse.T, precision=hi)
            columns.append((top, jnp.concatenate([diag, below], axis=0)))
        else:
            columns.append((top, diag))
    return columns, inverses


def right_solve(values, columns, inverses, block):
    hi = lax.Precision.HIGHEST
    parts = []
    for j, inverse in enumerate(inverses):
        top = j * block
        part = values[:, top:top + block]
        for k in range(j):
            c_top, col = columns[k]
            part = part - jnp.dot(parts[k], col[top - c_top:top - c_top + block].T, precision=hi)
        parts.append(jnp.dot(part, inverse.T, precision=hi))
    return jnp.concatenate(parts, axis=1)


def combine(earlier, later):
    return (earlier[0] * later[0], later[0][None, :] * earlier[1] + later[1])


def sketch_of(block_data, block_test):
    return lax.dot_general(
        block_data, block_test, (((0,), (0,)), ((), ())), preferred_element_type=jnp.float32
    )


def body(samples, test_matrix, forgetting, prior_sketch):
    block_data = samples[0]
    block_test = test_matrix[0]
    own_decay = forgetting[0, 0]
    prior_rows = prior_sketch[0].astype(jnp.float32)
    width = block_test.shape[1]
    rows = block_data.shape[1]
    steps = lax.axis_size("tm")
    place = lax.axis_index("tm")
    gathered = lax.all_gather(
        jnp.concatenate([block_data, block_test], axis=1), "tm", axis=0, tiled=True
    )
    all_data = gathered[:, :rows]
    all_test = gathered[:, rows:]
    decays = lax.all_gather(own_decay, "tm", axis=0)
    owner = lax.broadcasted_iota(jnp.int32, (steps, steps, 1), 0)
    later = lax.broadcasted_iota(jnp.int32, (steps, steps, 1), 1)
    inside = (later > owner) & (later <= place)
    weight = jnp.prod(jnp.where(inside, decays[None], 1.0), axis=1)
    weight = jnp.where(owner[:, 0] <= place, weight, 0.0)
    prior_weight = jnp.prod(jnp.where(later[0] <= place, decays, 1.0), axis=0)
    cols = block_test.shape[0]
    scaled = (all_test.reshape(steps, cols, width).astype(jnp.float32) * weight[:, None, :]).reshape(
        steps * cols, width
    )
    rounded = lax.reduce_precision(scaled, exponent_bits=8, mantissa_bits=7)
    high = rounded.astype(jnp.bfloat16)
    low = (scaled - rounded).astype(jnp.bfloat16)
    both = lax.dot_general(
        all_data,
        jnp.concatenate([high, low], axis=1),
        (((0,), (0,)), ((), ())),
        preferred_element_type=jnp.float32,
    )
    prefix = both[:, :width] + both[:, width:] + prior_weight[None, :] * prior_rows
    bins = lax.axis_size("bin")
    upward = [(i, i + 1) for i in range(bins - 1)]
    downward = [(b, a) for a, b in upward]
    sent = prefix.astype(jnp.bfloat16)
    below = lax.ppermute(sent, "bin", upward).astype(jnp.float32)
    above = lax.ppermute(sent, "bin", downward).astype(jnp.float32)
    mixed = prefix + 0.25 * (below + above)
    local_gram = lax.dot_general(
        mixed,
        mixed,
        (((0,), (0,)), ((), ())),
        precision=lax.Precision.HIGHEST,
        preferred_element_type=jnp.float32,
    )
    local_proj = jnp.dot(
        block_data.astype(jnp.float32),
        mixed,
        precision=lax.Precision.HIGHEST,
        preferred_element_type=jnp.float32,
    )
    summed = lax.psum(jnp.concatenate([local_gram, local_proj], axis=0), "rx")
    gram = summed[:width]
    block = 64
    columns, inverses = blocked_factor(gram, block)
    solved = right_solve(
        jnp.concatenate([mixed, summed[width:]], axis=0), columns, inverses, block
    )
    ortho = solved[:rows]
    coords = solved[rows:]
    receivers = rows * lax.axis_size("rx")
    basis = (math.sqrt(receivers) * ortho).astype(jnp.bfloat16)
    return (basis[None, None], coords[None])


def solution(mesh):
    return jax.shard_map(
        body,
        mesh=mesh,
        in_specs=(
            P("bin", "tm", "rx"),
            P("bin", "tm", None),
            P("bin", "tm", None),
            P("bin", "rx", None),
        ),
        out_specs=(P("bin", "tm", "rx", None), P("bin", "tm", None)),
        check_vma=False,
    )
```

```python
import math

import jax
import jax.numpy as jnp
from jax import lax
from jax.sharding import PartitionSpec as P


def prefix_2(part, axis, combine, identity):
    place = lax.axis_index(axis)
    gathered = jax.tree.map(lambda a: lax.all_gather(a, axis), part)
    state = jax.tree.map(lambda a, e: jnp.zeros_like(a) + jnp.asarray(e, a.dtype), part, identity)

    def one(hop, state):
        return combine(
            state, jax.tree.map(lambda a: lax.dynamic_index_in_dim(a, hop, 0, False), gathered)
        )

    return lax.fori_loop(0, place, one, state)


def with_halo(block, sides, width):
    for axis, dim in sides:
        count = lax.axis_size(axis)
        forward = [(i, i + 1) for i in range(count - 1)]
        backward = [(target, source) for source, target in forward]
        low = lax.ppermute(
            lax.slice_in_dim(block, block.shape[dim] - width, None, axis=dim), axis, forward
        )
        high = lax.ppermute(lax.slice_in_dim(block, 0, width, axis=dim), axis, backward)
        block = jnp.concatenate([low, block, high], axis=dim)
    return block


def lower_inverse(factor):
    hi = lax.Precision.HIGHEST
    size = factor.shape[0]
    scale = jnp.diagonal(factor)
    eye = jnp.eye(size, dtype=factor.dtype)
    nil = eye - factor / scale[:, None]
    power = nil
    total = eye + nil
    reach = 2
    while reach < size:
        power = jnp.dot(power, power, precision=hi)
        total = total + jnp.dot(total, power, precision=hi)
        reach *= 2
    return jnp.tril(total / scale[None, :])


def blocked_factor(gram, block):
    size = gram.shape[0]
    count = size // block
    hi = lax.Precision.HIGHEST
    eye = jnp.eye(block, dtype=gram.dtype)
    columns = []
    inverses = []
    for j in range(count):
        top, end = j * block, (j + 1) * block
        panel = gram[top:, top:end]
        if j:
            done = jnp.concatenate([c[top - c_top:] for c_top, c in columns], axis=1)
            panel = panel - jnp.dot(done, done[:block].T, precision=hi)
        diag = lax.linalg.cholesky(panel[:block], symmetrize_input=True)
        inverse = lower_inverse(diag)
        inverses.append(inverse)
        if j + 1 < count:
            below = jnp.dot(panel[block:], inverse.T, precision=hi)
            columns.append((top, jnp.concatenate([diag, below], axis=0)))
        else:
            columns.append((top, diag))
    return columns, inverses


def right_solve(values, columns, inverses, block):
    hi = lax.Precision.HIGHEST
    parts = []
    for j, inverse in enumerate(inverses):
        top = j * block
        part = values[:, top:top + block]
        for k in range(j):
            c_top, col = columns[k]
            part = part - jnp.dot(parts[k], col[top - c_top:top - c_top + block].T, precision=hi)
        parts.append(jnp.dot(part, inverse.T, precision=hi))
    return jnp.concatenate(parts, axis=1)


def combine(earlier, later):
    return (earlier[0] * later[0], later[0][None, :] * earlier[1] + later[1])


def sketch_of(block_data, block_test):
    return lax.dot_general(
        block_data, block_test, (((0,), (0,)), ((), ())), preferred_element_type=jnp.float32
    )


def body(samples, test_matrix, forgetting, prior_sketch):
    block_data = samples[0]
    block_test = test_matrix[0]
    own_decay = forgetting[0, 0]
    prior_rows = prior_sketch[0].astype(jnp.float32)
    width = block_test.shape[1]
    rows = block_data.shape[1]
    steps = lax.axis_size("tm")
    place = lax.axis_index("tm")
    gathered = lax.all_gather(
        jnp.concatenate([block_data, block_test], axis=1), "tm", axis=0, tiled=True
    )
    all_data = gathered[:, :rows]
    all_test = gathered[:, rows:]
    decays = lax.all_gather(own_decay, "tm", axis=0)
    owner = lax.broadcasted_iota(jnp.int32, (steps, steps, 1), 0)
    later = lax.broadcasted_iota(jnp.int32, (steps, steps, 1), 1)
    inside = (later > owner) & (later <= place)
    weight = jnp.prod(jnp.where(inside, decays[None], 1.0), axis=1)
    weight = jnp.where(owner[:, 0] <= place, weight, 0.0)
    prior_weight = jnp.prod(jnp.where(later[0] <= place, decays, 1.0), axis=0)
    cols = block_test.shape[0]
    scaled = (all_test.reshape(steps, cols, width).astype(jnp.float32) * weight[:, None, :]).reshape(
        steps * cols, width
    )
    rounded = lax.reduce_precision(scaled, exponent_bits=8, mantissa_bits=7)
    high = rounded.astype(jnp.bfloat16)
    low = (scaled - rounded).astype(jnp.bfloat16)
    both = lax.dot_general(
        all_data,
        jnp.concatenate([high, low], axis=1),
        (((0,), (0,)), ((), ())),
        preferred_element_type=jnp.float32,
    )
    prefix = both[:, :width] + both[:, width:] + prior_weight[None, :] * prior_rows
    bins = lax.axis_size("bin")
    upward = [(i, i + 1) for i in range(bins - 1)]
    downward = [(b, a) for a, b in upward]
    sent = prefix.astype(jnp.bfloat16)
    below = lax.ppermute(sent, "bin", upward).astype(jnp.float32)
    above = lax.ppermute(sent, "bin", downward).astype(jnp.float32)
    mixed = prefix + 0.25 * (below + above)
    local_gram = lax.dot_general(
        mixed,
        mixed,
        (((0,), (0,)), ((), ())),
        precision=lax.Precision.HIGHEST,
        preferred_element_type=jnp.float32,
    )
    local_proj = jnp.dot(
        block_data.astype(jnp.float32),
        mixed,
        precision=lax.Precision.HIGHEST,
        preferred_element_type=jnp.float32,
    )
    summed = lax.psum(jnp.concatenate([local_gram, local_proj], axis=0), "rx")
    gram = summed[:width]
    block = 128
    columns, inverses = blocked_factor(gram, block)
    solved = right_solve(
        jnp.concatenate([mixed, summed[width:]], axis=0), columns, inverses, block
    )
    ortho = solved[:rows]
    coords = solved[rows:]
    receivers = rows * lax.axis_size("rx")
    basis = (math.sqrt(receivers) * ortho).astype(jnp.bfloat16)
    return (basis[None, None], coords[None])


def solution(mesh):
    return jax.shard_map(
        body,
        mesh=mesh,
        in_specs=(
            P("bin", "tm", "rx"),
            P("bin", "tm", None),
            P("bin", "tm", None),
            P("bin", "rx", None),
        ),
        out_specs=(P("bin", "tm", "rx", None), P("bin", "tm", None)),
        check_vma=False,
    )
```

```python
import math

import jax
import jax.numpy as jnp
from jax import lax
from jax.sharding import PartitionSpec as P


def prefix_2(part, axis, combine, identity):
    place = lax.axis_index(axis)
    gathered = jax.tree.map(lambda a: lax.all_gather(a, axis), part)
    state = jax.tree.map(lambda a, e: jnp.zeros_like(a) + jnp.asarray(e, a.dtype), part, identity)

    def one(hop, state):
        return combine(
            state, jax.tree.map(lambda a: lax.dynamic_index_in_dim(a, hop, 0, False), gathered)
        )

    return lax.fori_loop(0, place, one, state)


def with_halo(block, sides, width):
    for axis, dim in sides:
        count = lax.axis_size(axis)
        forward = [(i, i + 1) for i in range(count - 1)]
        backward = [(target, source) for source, target in forward]
        low = lax.ppermute(
            lax.slice_in_dim(block, block.shape[dim] - width, None, axis=dim), axis, forward
        )
        high = lax.ppermute(lax.slice_in_dim(block, 0, width, axis=dim), axis, backward)
        block = jnp.concatenate([low, block, high], axis=dim)
    return block


def lower_inverse(factor):
    hi = lax.Precision.HIGHEST
    size = factor.shape[0]
    eye = jnp.eye(size, dtype=factor.dtype)
    scale = jnp.sum(factor * eye, axis=1)
    nil = eye - factor / scale[:, None]
    power = nil
    total = eye + nil
    reach = 2
    while reach < size:
        power = jnp.dot(power, power, precision=hi)
        total = total + jnp.dot(total, power, precision=hi)
        reach *= 2
    return jnp.tril(total / scale[None, :])


def blocked_factor(gram, block):
    size = gram.shape[0]
    count = size // block
    hi = lax.Precision.HIGHEST
    eye = jnp.eye(block, dtype=gram.dtype)
    columns = []
    inverses = []
    for j in range(count):
        top, end = j * block, (j + 1) * block
        panel = gram[top:, top:end]
        if j:
            done = jnp.concatenate([c[top - c_top:] for c_top, c in columns], axis=1)
            panel = panel - jnp.dot(done, done[:block].T, precision=hi)
        diag = lax.linalg.cholesky(panel[:block], symmetrize_input=False)
        inverse = lower_inverse(diag)
        inverses.append(inverse)
        if j + 1 < count:
            below = jnp.dot(panel[block:], inverse.T, precision=hi)
            columns.append((top, jnp.concatenate([diag, below], axis=0)))
        else:
            columns.append((top, diag))
    return columns, inverses


def right_solve(values, columns, inverses, block):
    hi = lax.Precision.HIGHEST
    parts = []
    for j, inverse in enumerate(inverses):
        top = j * block
        part = values[:, top:top + block]
        for k in range(j):
            c_top, col = columns[k]
            part = part - jnp.dot(parts[k], col[top - c_top:top - c_top + block].T, precision=hi)
        parts.append(jnp.dot(part, inverse.T, precision=hi))
    return jnp.concatenate(parts, axis=1)


def combine(earlier, later):
    return (earlier[0] * later[0], later[0][None, :] * earlier[1] + later[1])


def sketch_of(block_data, block_test):
    return lax.dot_general(
        block_data, block_test, (((0,), (0,)), ((), ())), preferred_element_type=jnp.float32
    )


def body(samples, test_matrix, forgetting, prior_sketch):
    block_data = samples[0]
    block_test = test_matrix[0]
    own_decay = forgetting[0, 0]
    prior_rows = prior_sketch[0].astype(jnp.float32)
    width = block_test.shape[1]
    rows = block_data.shape[1]
    steps = lax.axis_size("tm")
    place = lax.axis_index("tm")
    gathered = lax.all_gather(
        jnp.concatenate([block_data, block_test], axis=1), "tm", axis=0, tiled=True
    )
    all_data = gathered[:, :rows]
    all_test = gathered[:, rows:]
    decays = lax.all_gather(own_decay, "tm", axis=0)
    owner = lax.broadcasted_iota(jnp.int32, (steps, steps, 1), 0)
    later = lax.broadcasted_iota(jnp.int32, (steps, steps, 1), 1)
    inside = (later > owner) & (later <= place)
    weight = jnp.prod(jnp.where(inside, decays[None], 1.0), axis=1)
    weight = jnp.where(owner[:, 0] <= place, weight, 0.0)
    prior_weight = jnp.prod(jnp.where(later[0] <= place, decays, 1.0), axis=0)
    cols = block_test.shape[0]
    scaled = (all_test.reshape(steps, cols, width).astype(jnp.float32) * weight[:, None, :]).reshape(
        steps * cols, width
    )
    rounded = lax.reduce_precision(scaled, exponent_bits=8, mantissa_bits=7)
    high = rounded.astype(jnp.bfloat16)
    low = (scaled - rounded).astype(jnp.bfloat16)
    both = lax.dot_general(
        all_data,
        jnp.concatenate([high, low], axis=1),
        (((0,), (0,)), ((), ())),
        preferred_element_type=jnp.float32,
    )
    prefix = both[:, :width] + both[:, width:] + prior_weight[None, :] * prior_rows
    bins = lax.axis_size("bin")
    upward = [(i, i + 1) for i in range(bins - 1)]
    downward = [(b, a) for a, b in upward]
    sent = prefix.astype(jnp.bfloat16)
    below = lax.ppermute(sent, "bin", upward).astype(jnp.float32)
    above = lax.ppermute(sent, "bin", downward).astype(jnp.float32)
    mixed = prefix + 0.25 * (below + above)
    local_gram = lax.dot_general(
        mixed,
        mixed,
        (((0,), (0,)), ((), ())),
        precision=lax.Precision.HIGHEST,
        preferred_element_type=jnp.float32,
    )
    local_proj = jnp.dot(
        block_data.astype(jnp.float32),
        mixed,
        precision=lax.Precision.HIGHEST,
        preferred_element_type=jnp.float32,
    )
    summed = lax.psum(jnp.concatenate([local_gram, local_proj], axis=0), "rx")
    gram = summed[:width]
    block = 128
    columns, inverses = blocked_factor(gram, block)
    solved = right_solve(
        jnp.concatenate([mixed, summed[width:]], axis=0), columns, inverses, block
    )
    ortho = solved[:rows]
    coords = solved[rows:]
    receivers = rows * lax.axis_size("rx")
    basis = (math.sqrt(receivers) * ortho).astype(jnp.bfloat16)
    return (basis[None, None], coords[None])


def solution(mesh):
    return jax.shard_map(
        body,
        mesh=mesh,
        in_specs=(
            P("bin", "tm", "rx"),
            P("bin", "tm", None),
            P("bin", "tm", None),
            P("bin", "rx", None),
        ),
        out_specs=(P("bin", "tm", "rx", None), P("bin", "tm", None)),
        check_vma=False,
    )
```

```python
import math

import jax
import jax.numpy as jnp
from jax import lax
from jax.sharding import PartitionSpec as P


def prefix_2(part, axis, combine, identity):
    place = lax.axis_index(axis)
    gathered = jax.tree.map(lambda a: lax.all_gather(a, axis), part)
    state = jax.tree.map(lambda a, e: jnp.zeros_like(a) + jnp.asarray(e, a.dtype), part, identity)

    def one(hop, state):
        return combine(
            state, jax.tree.map(lambda a: lax.dynamic_index_in_dim(a, hop, 0, False), gathered)
        )

    return lax.fori_loop(0, place, one, state)


def with_halo(block, sides, width):
    for axis, dim in sides:
        count = lax.axis_size(axis)
        forward = [(i, i + 1) for i in range(count - 1)]
        backward = [(target, source) for source, target in forward]
        low = lax.ppermute(
            lax.slice_in_dim(block, block.shape[dim] - width, None, axis=dim), axis, forward
        )
        high = lax.ppermute(lax.slice_in_dim(block, 0, width, axis=dim), axis, backward)
        block = jnp.concatenate([low, block, high], axis=dim)
    return block


def lower_inverse(factor):
    hi = lax.Precision.HIGHEST
    size = factor.shape[0]
    eye = jnp.eye(size, dtype=factor.dtype)
    scale = jnp.sum(factor * eye, axis=1)
    nil = eye - factor / scale[:, None]
    power = nil
    total = eye + nil
    reach = 2
    while reach < size:
        power = jnp.dot(power, power, precision=hi)
        total = total + jnp.dot(total, power, precision=hi)
        reach *= 2
    return jnp.tril(total / scale[None, :])


def blocked_factor(gram, block):
    size = gram.shape[0]
    count = size // block
    hi = lax.Precision.HIGHEST
    eye = jnp.eye(block, dtype=gram.dtype)
    columns = []
    inverses = []
    for j in range(count):
        top, end = j * block, (j + 1) * block
        panel = gram[top:, top:end]
        if j:
            done = jnp.concatenate([c[top - c_top:] for c_top, c in columns], axis=1)
            panel = panel - jnp.dot(done, done[:block].T, precision=hi)
        diag = lax.linalg.cholesky(panel[:block], symmetrize_input=False)
        inverse = lower_inverse(diag)
        inverses.append(inverse)
        if j + 1 < count:
            below = jnp.dot(panel[block:], inverse.T, precision=hi)
            columns.append((top, jnp.concatenate([diag, below], axis=0)))
        else:
            columns.append((top, diag))
    return columns, inverses


def right_solve(values, columns, inverses, block):
    hi = lax.Precision.HIGHEST
    parts = []
    for j, inverse in enumerate(inverses):
        top = j * block
        part = values[:, top:top + block]
        for k in range(j):
            c_top, col = columns[k]
            part = part - jnp.dot(parts[k], col[top - c_top:top - c_top + block].T, precision=hi)
        parts.append(jnp.dot(part, inverse.T, precision=hi))
    return jnp.concatenate(parts, axis=1)


def combine(earlier, later):
    return (earlier[0] * later[0], later[0][None, :] * earlier[1] + later[1])


def sketch_of(block_data, block_test):
    return lax.dot_general(
        block_data, block_test, (((0,), (0,)), ((), ())), preferred_element_type=jnp.float32
    )


def body(samples, test_matrix, forgetting, prior_sketch):
    block_data = samples[0]
    block_test = test_matrix[0]
    own_decay = forgetting[0, 0]
    prior_rows = prior_sketch[0].astype(jnp.float32)
    width = block_test.shape[1]
    rows = block_data.shape[1]
    steps = lax.axis_size("tm")
    place = lax.axis_index("tm")
    all_data, all_test = lax.all_gather((block_data, block_test), "tm", axis=0, tiled=True)
    decays = lax.all_gather(own_decay, "tm", axis=0)
    owner = lax.broadcasted_iota(jnp.int32, (steps, steps, 1), 0)
    later = lax.broadcasted_iota(jnp.int32, (steps, steps, 1), 1)
    inside = (later > owner) & (later <= place)
    weight = jnp.prod(jnp.where(inside, decays[None], 1.0), axis=1)
    weight = jnp.where(owner[:, 0] <= place, weight, 0.0)
    prior_weight = jnp.prod(jnp.where(later[0] <= place, decays, 1.0), axis=0)
    cols = block_test.shape[0]
    scaled = (all_test.reshape(steps, cols, width).astype(jnp.float32) * weight[:, None, :]).reshape(
        steps * cols, width
    )
    rounded = lax.reduce_precision(scaled, exponent_bits=8, mantissa_bits=7)
    high = rounded.astype(jnp.bfloat16)
    low = (scaled - rounded).astype(jnp.bfloat16)
    both = lax.dot_general(
        all_data,
        jnp.concatenate([high, low], axis=1),
        (((0,), (0,)), ((), ())),
        preferred_element_type=jnp.float32,
    )
    prefix = both[:, :width] + both[:, width:] + prior_weight[None, :] * prior_rows
    bins = lax.axis_size("bin")
    upward = [(i, i + 1) for i in range(bins - 1)]
    downward = [(b, a) for a, b in upward]
    sent = prefix.astype(jnp.bfloat16)
    below = lax.ppermute(sent, "bin", upward).astype(jnp.float32)
    above = lax.ppermute(sent, "bin", downward).astype(jnp.float32)
    mixed = prefix + 0.25 * (below + above)
    local_gram = lax.dot_general(
        mixed,
        mixed,
        (((0,), (0,)), ((), ())),
        precision=lax.Precision.HIGHEST,
        preferred_element_type=jnp.float32,
    )
    local_proj = jnp.dot(
        block_data.astype(jnp.float32),
        mixed,
        precision=lax.Precision.HIGHEST,
        preferred_element_type=jnp.float32,
    )
    summed = lax.psum(jnp.concatenate([local_gram, local_proj], axis=0), "rx")
    gram = summed[:width]
    block = 128
    columns, inverses = blocked_factor(gram, block)
    solved = right_solve(
        jnp.concatenate([mixed, summed[width:]], axis=0), columns, inverses, block
    )
    ortho = solved[:rows]
    coords = solved[rows:]
    receivers = rows * lax.axis_size("rx")
    basis = (math.sqrt(receivers) * ortho).astype(jnp.bfloat16)
    return (basis[None, None], coords[None])


def solution(mesh):
    return jax.shard_map(
        body,
        mesh=mesh,
        in_specs=(
            P("bin", "tm", "rx"),
            P("bin", "tm", None),
            P("bin", "tm", None),
            P("bin", "rx", None),
        ),
        out_specs=(P("bin", "tm", "rx", None), P("bin", "tm", None)),
        check_vma=False,
    )
```

```python
import math

import jax
import jax.numpy as jnp
from jax import lax
from jax.sharding import PartitionSpec as P


def prefix_2(part, axis, combine, identity):
    place = lax.axis_index(axis)
    gathered = jax.tree.map(lambda a: lax.all_gather(a, axis), part)
    state = jax.tree.map(lambda a, e: jnp.zeros_like(a) + jnp.asarray(e, a.dtype), part, identity)

    def one(hop, state):
        return combine(
            state, jax.tree.map(lambda a: lax.dynamic_index_in_dim(a, hop, 0, False), gathered)
        )

    return lax.fori_loop(0, place, one, state)


def with_halo(block, sides, width):
    for axis, dim in sides:
        count = lax.axis_size(axis)
        forward = [(i, i + 1) for i in range(count - 1)]
        backward = [(target, source) for source, target in forward]
        low = lax.ppermute(
            lax.slice_in_dim(block, block.shape[dim] - width, None, axis=dim), axis, forward
        )
        high = lax.ppermute(lax.slice_in_dim(block, 0, width, axis=dim), axis, backward)
        block = jnp.concatenate([low, block, high], axis=dim)
    return block


def lower_inverse(factor):
    hi = lax.Precision.HIGH
    size = factor.shape[0]
    eye = jnp.eye(size, dtype=factor.dtype)
    scale = jnp.sum(factor * eye, axis=1)
    nil = eye - factor / scale[:, None]
    power = nil
    total = eye + nil
    reach = 2
    while reach < size:
        power = jnp.dot(power, power, precision=hi)
        total = total + jnp.dot(total, power, precision=hi)
        reach *= 2
    return jnp.tril(total / scale[None, :])


def blocked_factor(gram, block):
    size = gram.shape[0]
    count = size // block
    hi = lax.Precision.HIGH
    eye = jnp.eye(block, dtype=gram.dtype)
    columns = []
    inverses = []
    for j in range(count):
        top, end = j * block, (j + 1) * block
        panel = gram[top:, top:end]
        if j:
            done = jnp.concatenate([c[top - c_top:] for c_top, c in columns], axis=1)
            panel = panel - jnp.dot(done, done[:block].T, precision=hi)
        diag = lax.linalg.cholesky(panel[:block], symmetrize_input=False)
        inverse = lower_inverse(diag)
        inverses.append(inverse)
        if j + 1 < count:
            below = jnp.dot(panel[block:], inverse.T, precision=hi)
            columns.append((top, jnp.concatenate([diag, below], axis=0)))
        else:
            columns.append((top, diag))
    return columns, inverses


def right_solve(values, columns, inverses, block):
    hi = lax.Precision.HIGH
    parts = []
    for j, inverse in enumerate(inverses):
        top = j * block
        part = values[:, top:top + block]
        for k in range(j):
            c_top, col = columns[k]
            part = part - jnp.dot(parts[k], col[top - c_top:top - c_top + block].T, precision=hi)
        parts.append(jnp.dot(part, inverse.T, precision=hi))
    return jnp.concatenate(parts, axis=1)


def combine(earlier, later):
    return (earlier[0] * later[0], later[0][None, :] * earlier[1] + later[1])


def sketch_of(block_data, block_test):
    return lax.dot_general(
        block_data, block_test, (((0,), (0,)), ((), ())), preferred_element_type=jnp.float32
    )


def body(samples, test_matrix, forgetting, prior_sketch):
    block_data = samples[0]
    block_test = test_matrix[0]
    own_decay = forgetting[0, 0]
    prior_rows = prior_sketch[0].astype(jnp.float32)
    width = block_test.shape[1]
    rows = block_data.shape[1]
    steps = lax.axis_size("tm")
    place = lax.axis_index("tm")
    gathered = lax.all_gather(
        jnp.concatenate([block_data, block_test], axis=1), "tm", axis=0, tiled=True
    )
    all_data = gathered[:, :rows]
    all_test = gathered[:, rows:]
    decays = lax.all_gather(own_decay, "tm", axis=0)
    owner = lax.broadcasted_iota(jnp.int32, (steps, steps, 1), 0)
    later = lax.broadcasted_iota(jnp.int32, (steps, steps, 1), 1)
    inside = (later > owner) & (later <= place)
    weight = jnp.prod(jnp.where(inside, decays[None], 1.0), axis=1)
    weight = jnp.where(owner[:, 0] <= place, weight, 0.0)
    prior_weight = jnp.prod(jnp.where(later[0] <= place, decays, 1.0), axis=0)
    cols = block_test.shape[0]
    scaled = (all_test.reshape(steps, cols, width).astype(jnp.float32) * weight[:, None, :]).reshape(
        steps * cols, width
    )
    rounded = lax.reduce_precision(scaled, exponent_bits=8, mantissa_bits=7)
    high = rounded.astype(jnp.bfloat16)
    low = (scaled - rounded).astype(jnp.bfloat16)
    both = lax.dot_general(
        all_data,
        jnp.concatenate([high, low], axis=1),
        (((0,), (0,)), ((), ())),
        preferred_element_type=jnp.float32,
    )
    prefix = both[:, :width] + both[:, width:] + prior_weight[None, :] * prior_rows
    bins = lax.axis_size("bin")
    upward = [(i, i + 1) for i in range(bins - 1)]
    downward = [(b, a) for a, b in upward]
    sent = prefix.astype(jnp.bfloat16)
    below = lax.ppermute(sent, "bin", upward).astype(jnp.float32)
    above = lax.ppermute(sent, "bin", downward).astype(jnp.float32)
    mixed = prefix + 0.25 * (below + above)
    local_gram = lax.dot_general(
        mixed,
        mixed,
        (((0,), (0,)), ((), ())),
        precision=lax.Precision.HIGHEST,
        preferred_element_type=jnp.float32,
    )
    local_proj = jnp.dot(
        block_data.astype(jnp.float32),
        mixed,
        precision=lax.Precision.HIGHEST,
        preferred_element_type=jnp.float32,
    )
    summed = lax.psum(jnp.concatenate([local_gram, local_proj], axis=0), "rx")
    gram = summed[:width]
    block = 128
    columns, inverses = blocked_factor(gram, block)
    solved = right_solve(
        jnp.concatenate([mixed, summed[width:]], axis=0), columns, inverses, block
    )
    ortho = solved[:rows]
    coords = solved[rows:]
    receivers = rows * lax.axis_size("rx")
    basis = (math.sqrt(receivers) * ortho).astype(jnp.bfloat16)
    return (basis[None, None], coords[None])


def solution(mesh):
    return jax.shard_map(
        body,
        mesh=mesh,
        in_specs=(
            P("bin", "tm", "rx"),
            P("bin", "tm", None),
            P("bin", "tm", None),
            P("bin", "rx", None),
        ),
        out_specs=(P("bin", "tm", "rx", None), P("bin", "tm", None)),
        check_vma=False,
    )
```
